256 devices in a mesh: dp: 32 (over z_lo, y, x), tensor: 8 (over z_hi, core).
Axes of the slice: x: 4, y: 4, z: 8 (z_hi: 4, z_lo: 2; z = z_hi * 2 + z_lo), core: 2. Of those that a mesh axis runs over, the one named last changes fastest.
Arguments:
- embeds: bfloat16 [512, 4608], P('dp'), may hold values from -6 to 6
- owner: int32 [64, 8], P('dp'), may hold values from 0 to 7, each once within a row
- pairs: int32 [64, 56, 2], P('dp'), may hold values from 0 to 7, as said below
- pref_weight: bfloat16 [2, 4608, 4608], P(None, 'dp', 'tensor'), may hold values from -0.0625 to 0.0625
- pref_bias: float32 [4608], P('tensor'), may hold values from -3 to 3
- pref_out: float32 [4608], P('tensor'), may hold values from -0.375 to 0.375
- logratio: float32 [512], P('dp'), may hold values from -3 to 3
- attn_out: bfloat16 [32768, 4096], P('dp', 'tensor'), may hold values from -6 to 6
- grad_out: bfloat16 [32768, 4608], P('dp', 'tensor'), may hold values from -6 to 6
- w_out: bfloat16 [4608, 4096], P('dp', 'tensor'), may hold values from -0.09375 to 0.09375
Outputs:
- d_attn: bfloat16 [32768, 4096], P('dp', 'tensor')
- o_grad: float32 [4608, 4096], P('dp', 'tensor')
The draws below stay inside these ranges and needn't reach their ends.
Inputs may be any that keep to these rules, and one draw needn't show every extreme that they name: `pairs`: the two numbers of a pair differ. Each row of owner names every number once.
All inputs are finite; a program needn't handle non-finite values.
Results may differ from the reference program's by a relative error of at most 0.0049.
Values may be sent and summed in bfloat16 or wider, within the bound.
No kernel may reach another device: no remote copies, remote signals or barrier semaphores. Data moves between devices by JAX's collectives and lax.ppermute only.
A program may use at most 128 MiB of HBM per device.

```python
import jax
import jax.numpy as jnp

D = 4608
HID = 4096
PH = 4608
K = 8
NPAIR = 56
L = 64
PROMPTS = 64
RESP = 512
TOKENS = 32768


def draw_pairs(key, part):
    first_key = jax.random.fold_in(key, 11)
    step_key = jax.random.fold_in(key, 12)
    first = jax.random.randint(first_key, (PROMPTS, NPAIR), 0, K)
    step = jax.random.randint(step_key, (PROMPTS, NPAIR), 1, K)
    second = (first + step) % K
    return jnp.stack([first, second], axis=-1).astype(jnp.int32)


def block_levels(stream_key, extent, pieces, low, largest):
    factor_of, own = 1.0, jax.random.fold_in(stream_key, 6)
    for position, blocks in pieces:
        steps = jnp.exp(jax.random.uniform(jax.random.fold_in(own, position), (blocks,), jnp.float32, low / len(pieces), largest / len(pieces)))
        factor_of = factor_of * jnp.repeat(steps, extent[position] // blocks).reshape([-1 if axis == position else 1 for axis in range(len(extent))])
    return factor_of


def bell_draw(key, dims, width, limit, cuts=(), held_as=jnp.bfloat16):
    drawn = width * jax.random.normal(key, dims, jnp.float32)
    if cuts:
        drawn = drawn * block_levels(key, dims, cuts, -0.22, 0.18)
    return jnp.clip(drawn, -limit, limit).astype(held_as)


def setup_inputs(seed: int = 0) -> dict:
    key_of = jax.random.split(jax.random.key(seed), 11)
    return {
        "embeds": bell_draw(key_of[0], (RESP, D), 1.0, 6.0, ((0, 32),)),
        "owner": jax.vmap(lambda own: jax.random.permutation(own, K))(jax.random.split(key_of[1], PROMPTS)).reshape((PROMPTS, K)).astype(jnp.int32),
        "pairs": draw_pairs(jax.random.fold_in(key_of[10], 71), 0),
        "pref_weight": bell_draw(key_of[3], (2, D, PH), (2 * D) ** -0.5, 0.0625, ((1, 32), (2, 8))),
        "pref_bias": bell_draw(key_of[4], (PH,), 0.5, 3.0, ((0, 8),), jnp.float32),
        "pref_out": bell_draw(key_of[5], (PH,), (PH // 16) ** -0.5, 0.375, ((0, 8),), jnp.float32),
        "logratio": bell_draw(key_of[6], (RESP,), 0.5, 3.0, ((0, 32),), jnp.float32),
        "attn_out": bell_draw(key_of[7], (TOKENS, HID), 1.0, 6.0, ((0, 32), (1, 8))),
        "grad_out": bell_draw(key_of[8], (TOKENS, D), 1.0, 6.0, ((0, 32), (1, 8))),
        "w_out": bell_draw(key_of[9], (D, HID), HID ** -0.5, 0.09375, ((0, 32), (1, 8))),
    }


eta_scale = 2.0


def reference(embeds, owner, pairs, pref_weight, pref_bias, pref_out, logratio, attn_out, grad_out, w_out):
    upper = jnp.dot(embeds, pref_weight[0], preferred_element_type=jnp.float32)
    lower = jnp.dot(embeds, pref_weight[1], preferred_element_type=jnp.float32)
    prompts = owner.shape[0]
    base = (jnp.arange(prompts, dtype=jnp.int32) * K)[:, None]
    row_a = base + jnp.take_along_axis(owner, pairs[:, :, 0], axis=1)
    row_b = base + jnp.take_along_axis(owner, pairs[:, :, 1], axis=1)
    pre = upper[row_a] + lower[row_b] + pref_bias
    hidden = jax.nn.gelu(pre)
    logit = jnp.sum(hidden * pref_out, axis=-1)
    prob = jax.nn.sigmoid(logit)
    numbers = jnp.arange(K, dtype=jnp.int32)
    first = (pairs[:, :, 0][:, :, None] == numbers).astype(jnp.float32)
    second = (pairs[:, :, 1][:, :, None] == numbers).astype(jnp.float32)
    wins = jnp.sum(prob[:, :, None] * first + (1.0 - prob)[:, :, None] * second, axis=1)
    count = jnp.sum(first + second, axis=1)
    winrate = (wins + 1.0) / (count + 2.0)
    placed = (owner[:, :, None] == numbers).astype(jnp.float32)
    rowrate = jnp.sum(winrate[:, :, None] * placed, axis=1).reshape(-1)
    coef = 2.0 * (logratio - eta_scale * (rowrate - 0.5))
    resp = coef.shape[0]
    weighted = (grad_out.astype(jnp.float32).reshape(resp, L, -1) * coef[:, None, None]).reshape(grad_out.shape).astype(jnp.bfloat16)
    d_attn = jnp.dot(weighted, w_out, preferred_element_type=jnp.float32).astype(jnp.bfloat16)
    o_grad = jnp.dot(weighted.T, attn_out, preferred_element_type=jnp.float32) / resp
    return d_attn, o_grad
```

```python
import jax
import jax.numpy as jnp
from jax import lax
from jax.sharding import PartitionSpec as P

eta_scale = 2.0


def shards(
    embeds, owner, pairs, pref_weight, pref_bias, pref_out, logratio, attn_out, grad_out, w_out
):
    resp_dev = embeds.shape[0]
    prompts_dev = owner.shape[0]
    groups = owner.shape[1]
    npairs = pairs.shape[1]
    width_local = pref_weight.shape[2]
    n_dp = lax.axis_size("dp")
    features = lax.all_gather(grad_out, "tensor", axis=1, tiled=True)
    cols = lax.all_to_all(embeds, "dp", 1, 0, tiled=True)
    part = jnp.concatenate(
        [
            jnp.dot(cols, pref_weight[0], preferred_element_type=jnp.float32),
            jnp.dot(cols, pref_weight[1], preferred_element_type=jnp.float32),
        ],
        axis=1,
    )
    part = part.reshape(n_dp, resp_dev, part.shape[1])
    proj = jnp.sum(lax.all_to_all(part, "dp", 0, 0, tiled=True), axis=0)
    base = (jnp.arange(prompts_dev, dtype=jnp.int32) * groups)[:, None]
    row_a = base + jnp.take_along_axis(owner, pairs[:, :, 0], axis=1)
    row_b = base + jnp.take_along_axis(owner, pairs[:, :, 1], axis=1)
    upper = proj[:, :width_local][row_a.reshape(-1)]
    lower = proj[:, width_local:][row_b.reshape(-1)]
    pre = (upper + lower).reshape(prompts_dev, npairs, width_local)
    hidden = jax.nn.gelu(pre + pref_bias)
    partial_logit = jnp.sum(hidden * pref_out, axis=-1)
    logit = lax.psum(partial_logit, "tensor")
    prob = jax.nn.sigmoid(logit)
    numbers = jnp.arange(groups, dtype=jnp.int32)
    first = (pairs[:, :, 0][:, :, None] == numbers).astype(jnp.float32)
    second = (pairs[:, :, 1][:, :, None] == numbers).astype(jnp.float32)
    wins = jnp.sum(prob[:, :, None] * first + (1.0 - prob)[:, :, None] * second, axis=1)
    count = jnp.sum(first + second, axis=1)
    winrate = (wins + 1.0) / (count + 2.0)
    placed = (owner[:, :, None] == numbers).astype(jnp.float32)
    rowrate = jnp.sum(winrate[:, :, None] * placed, axis=1).reshape(-1)
    coef = 2.0 * (logratio - eta_scale * (rowrate - 0.5))
    weighted = (
        (
            features.astype(jnp.float32).reshape(resp_dev, -1, features.shape[1])
            * coef[:, None, None]
        )
        .reshape(features.shape)
        .astype(jnp.bfloat16)
    )
    copies = jnp.broadcast_to(w_out[None], (n_dp,) + w_out.shape)
    piece = lax.all_to_all(copies, "dp", 0, 0, tiled=True).reshape(-1, w_out.shape[1])
    d_attn = jnp.dot(weighted, piece, preferred_element_type=jnp.float32).astype(jnp.bfloat16)
    total_resp = resp_dev * n_dp
    full = lax.dot_general(
        weighted, attn_out, (((0,), (0,)), ((), ())), preferred_element_type=jnp.float32
    )
    full = full.astype(jnp.bfloat16).reshape(n_dp, -1, full.shape[1])
    shares = lax.all_to_all(full, "dp", 0, 0, tiled=True)
    o_grad = jnp.sum(shares.astype(jnp.float32), axis=0) / total_resp
    return (d_attn, o_grad)


def solution(mesh):
    return jax.shard_map(
        shards,
        mesh=mesh,
        in_specs=(
            P("dp", None),
            P("dp", None),
            P("dp", None, None),
            P(None, "dp", "tensor"),
            P("tensor"),
            P("tensor"),
            P("dp"),
            P("dp", "tensor"),
            P("dp", "tensor"),
            P("dp", "tensor"),
        ),
        out_specs=(P("dp", "tensor"), P("dp", "tensor")),
        check_vma=False,
    )
```

```python
import jax
import jax.numpy as jnp
from jax import lax
from jax.sharding import Mesh
from jax.sharding import PartitionSpec as P

eta_scale = 2.0

DP = ("zl", "y", "x")
TP = ("zh", "c")
PLANE = ("y", "x")


def shards(
    embeds, owner, pairs, pref_weight, pref_bias, pref_out, logratio, attn_out, grad_out, w_out
):
    resp_dev = embeds.shape[0]
    prompts_dev = owner.shape[0]
    groups = owner.shape[1]
    npairs = pairs.shape[1]
    width_local = pref_weight.shape[2]
    rows_w = pref_weight.shape[1]
    n_dp = lax.axis_size(DP)
    n_zl = lax.axis_size("zl")
    n_plane = lax.axis_size(PLANE)
    features = lax.all_gather(grad_out, TP, axis=1, tiled=True)
    copies = jnp.broadcast_to(w_out[None], (n_dp,) + w_out.shape)
    piece = lax.all_to_all(copies, DP, 0, 0, tiled=True).reshape(-1, w_out.shape[1])

    zl = lax.axis_index("zl")
    other = lax.ppermute(pref_weight, "zl", [(k, (k + 1) % n_zl) for k in range(n_zl)])
    pair_w = jnp.where(
        zl == 0,
        jnp.concatenate([pref_weight, other], axis=1),
        jnp.concatenate([other, pref_weight], axis=1),
    )
    cols = embeds.reshape(resp_dev, n_zl, n_plane, rows_w).transpose(2, 0, 1, 3)
    cols = lax.all_to_all(cols, PLANE, 0, 0, tiled=True).reshape(n_plane * resp_dev, n_zl * rows_w)
    part = jnp.concatenate(
        [
            jnp.dot(cols, pair_w[0], preferred_element_type=jnp.float32),
            jnp.dot(cols, pair_w[1], preferred_element_type=jnp.float32),
        ],
        axis=1,
    )
    part = part.reshape(n_plane, resp_dev, part.shape[1])
    proj = jnp.sum(lax.all_to_all(part, PLANE, 0, 0, tiled=True), axis=0)

    base = (jnp.arange(prompts_dev, dtype=jnp.int32) * groups)[:, None]
    row_a = base + jnp.take_along_axis(owner, pairs[:, :, 0], axis=1)
    row_b = base + jnp.take_along_axis(owner, pairs[:, :, 1], axis=1)
    upper = proj[:, :width_local][row_a.reshape(-1)]
    lower = proj[:, width_local:][row_b.reshape(-1)]
    pre = (upper + lower).reshape(prompts_dev, npairs, width_local)
    hidden = jax.nn.gelu(pre + pref_bias)
    partial_logit = jnp.sum(hidden * pref_out, axis=-1)
    logit = lax.psum(partial_logit, TP)
    prob = jax.nn.sigmoid(logit)
    numbers = jnp.arange(groups, dtype=jnp.int32)
    first = (pairs[:, :, 0][:, :, None] == numbers).astype(jnp.float32)
    second = (pairs[:, :, 1][:, :, None] == numbers).astype(jnp.float32)
    wins = jnp.sum(prob[:, :, None] * first + (1.0 - prob)[:, :, None] * second, axis=1)
    count = jnp.sum(first + second, axis=1)
    winrate = (wins + 1.0) / (count + 2.0)
    placed = (owner[:, :, None] == numbers).astype(jnp.float32)
    rowrate = jnp.sum(winrate[:, :, None] * placed, axis=1).reshape(-1)
    coef = 2.0 * (logratio - eta_scale * (rowrate - 0.5))
    weighted = (
        (
            features.astype(jnp.float32).reshape(resp_dev, -1, features.shape[1])
            * coef[:, None, None]
        )
        .reshape(features.shape)
        .astype(jnp.bfloat16)
    )
    total_resp = resp_dev * n_dp
    full = lax.dot_general(
        weighted, attn_out, (((0,), (0,)), ((), ())), preferred_element_type=jnp.float32
    )
    full = full.astype(jnp.bfloat16).reshape(n_dp, -1, full.shape[1])
    shares = lax.all_to_all(full, DP, 0, 0, tiled=True)
    d_attn = jnp.dot(weighted, piece, preferred_element_type=jnp.float32).astype(jnp.bfloat16)
    o_grad = jnp.sum(shares.astype(jnp.float32), axis=0) / total_resp
    return (d_attn, o_grad)


def solution(mesh):
    n_zl = 2
    fine = Mesh(
        mesh.devices.reshape(
            n_zl, mesh.shape["dp"] // (n_zl * 4), 4, mesh.shape["tensor"] // 2, 2
        ),
        ("zl", "y", "x", "zh", "c"),
    )
    return jax.shard_map(
        shards,
        mesh=fine,
        in_specs=(
            P(DP, None),
            P(DP, None),
            P(DP, None, None),
            P(None, DP, TP),
            P(TP),
            P(TP),
            P(DP),
            P(DP, TP),
            P(DP, TP),
            P(DP, TP),
        ),
        out_specs=(P(DP, TP), P(DP, TP)),
        check_vma=False,
    )
```

```python
import jax
import jax.numpy as jnp
from jax import lax
from jax.sharding import Mesh
from jax.sharding import PartitionSpec as P

eta_scale = 2.0

DP = ("zl", "y", "x")
TP = ("zh", "c")
PLANE = ("y", "x")


def shards(
    embeds, owner, pairs, pref_weight, pref_bias, pref_out, logratio, attn_out, grad_out, w_out
):
    resp_dev = embeds.shape[0]
    prompts_dev = owner.shape[0]
    groups = owner.shape[1]
    npairs = pairs.shape[1]
    width_local = pref_weight.shape[2]
    rows_w = pref_weight.shape[1]
    n_dp = lax.axis_size(DP)
    n_zl = lax.axis_size("zl")
    n_plane = lax.axis_size(PLANE)
    features = lax.all_gather(grad_out, TP, axis=1, tiled=True)

    zl = lax.axis_index("zl")
    other = lax.ppermute(pref_weight, "zl", [(k, (k + 1) % n_zl) for k in range(n_zl)])
    pair_w = jnp.where(
        zl == 0,
        jnp.concatenate([pref_weight, other], axis=1),
        jnp.concatenate([other, pref_weight], axis=1),
    )
    cols = embeds.reshape(resp_dev, n_zl, n_plane, rows_w).transpose(2, 0, 1, 3)
    cols = lax.all_to_all(cols, PLANE, 0, 0, tiled=True).reshape(n_plane * resp_dev, n_zl * rows_w)
    part = jnp.concatenate(
        [
            jnp.dot(cols, pair_w[0], preferred_element_type=jnp.float32),
            jnp.dot(cols, pair_w[1], preferred_element_type=jnp.float32),
        ],
        axis=1,
    )
    part = part.reshape(n_plane, resp_dev, part.shape[1])
    proj = jnp.sum(lax.all_to_all(part, PLANE, 0, 0, tiled=True), axis=0)

    base = (jnp.arange(prompts_dev, dtype=jnp.int32) * groups)[:, None]
    row_a = base + jnp.take_along_axis(owner, pairs[:, :, 0], axis=1)
    row_b = base + jnp.take_along_axis(owner, pairs[:, :, 1], axis=1)
    upper = proj[:, :width_local][row_a.reshape(-1)]
    lower = proj[:, width_local:][row_b.reshape(-1)]
    pre = (upper + lower).reshape(prompts_dev, npairs, width_local)
    hidden = jax.nn.gelu(pre + pref_bias)
    partial_logit = jnp.sum(hidden * pref_out, axis=-1)
    logit = lax.psum(partial_logit, TP)
    copies = jnp.broadcast_to(w_out[None], (n_dp,) + w_out.shape)
    copies, logit = lax.optimization_barrier((copies, logit))
    piece = lax.all_to_all(copies, DP, 0, 0, tiled=True).reshape(-1, w_out.shape[1])
    prob = jax.nn.sigmoid(logit)
    numbers = jnp.arange(groups, dtype=jnp.int32)
    first = (pairs[:, :, 0][:, :, None] == numbers).astype(jnp.float32)
    second = (pairs[:, :, 1][:, :, None] == numbers).astype(jnp.float32)
    wins = jnp.sum(prob[:, :, None] * first + (1.0 - prob)[:, :, None] * second, axis=1)
    count = jnp.sum(first + second, axis=1)
    winrate = (wins + 1.0) / (count + 2.0)
    placed = (owner[:, :, None] == numbers).astype(jnp.float32)
    rowrate = jnp.sum(winrate[:, :, None] * placed, axis=1).reshape(-1)
    coef = 2.0 * (logratio - eta_scale * (rowrate - 0.5))
    weighted = (
        (
            features.astype(jnp.float32).reshape(resp_dev, -1, features.shape[1])
            * coef[:, None, None]
        )
        .reshape(features.shape)
        .astype(jnp.bfloat16)
    )
    total_resp = resp_dev * n_dp
    full = lax.dot_general(
        weighted, attn_out, (((0,), (0,)), ((), ())), preferred_element_type=jnp.float32
    )
    full = full.astype(jnp.bfloat16).reshape(n_dp, -1, full.shape[1])
    shares = lax.all_to_all(full, DP, 0, 0, tiled=True)
    d_attn = jnp.dot(weighted, piece, preferred_element_type=jnp.float32).astype(jnp.bfloat16)
    o_grad = jnp.sum(shares.astype(jnp.float32), axis=0) / total_resp
    return (d_attn, o_grad)


def solution(mesh):
    n_zl = 2
    fine = Mesh(
        mesh.devices.reshape(
            n_zl, mesh.shape["dp"] // (n_zl * 4), 4, mesh.shape["tensor"] // 2, 2
        ),
        ("zl", "y", "x", "zh", "c"),
    )
    return jax.shard_map(
        shards,
        mesh=fine,
        in_specs=(
            P(DP, None),
            P(DP, None),
            P(DP, None, None),
            P(None, DP, TP),
            P(TP),
            P(TP),
            P(DP),
            P(DP, TP),
            P(DP, TP),
            P(DP, TP),
        ),
        out_specs=(P(DP, TP), P(DP, TP)),
        check_vma=False,
    )
```

```python
import jax
import jax.numpy as jnp
from jax import lax
from jax.sharding import Mesh
from jax.sharding import PartitionSpec as P

eta_scale = 2.0

DP = ("zl", "y", "x")
TP = ("zh", "c")
PLANE = ("y", "x")


def shards(
    embeds, owner, pairs, pref_weight, pref_bias, pref_out, logratio, attn_out, grad_out, w_out
):
    resp_dev = embeds.shape[0]
    prompts_dev = owner.shape[0]
    groups = owner.shape[1]
    npairs = pairs.shape[1]
    width_local = pref_weight.shape[2]
    rows_w = pref_weight.shape[1]
    n_dp = lax.axis_size(DP)
    n_zl = lax.axis_size("zl")
    n_plane = lax.axis_size(PLANE)
    features = lax.all_gather(grad_out, TP, axis=1, tiled=True)
    zl = lax.axis_index("zl")
    swap = [(k, (k + 1) % n_zl) for k in range(n_zl)]
    w_other = lax.ppermute(w_out, "zl", swap)
    w_pair = jnp.where(zl == 0, jnp.stack([w_out, w_other]), jnp.stack([w_other, w_out]))
    copies = jnp.broadcast_to(w_pair[None], (n_plane,) + w_pair.shape)
    piece = lax.all_to_all(copies, PLANE, 0, 0, tiled=True)
    piece = piece.transpose(1, 0, 2, 3).reshape(-1, w_out.shape[1])

    other = lax.ppermute(pref_weight, "zl", swap)
    pair_w = jnp.where(
        zl == 0,
        jnp.concatenate([pref_weight, other], axis=1),
        jnp.concatenate([other, pref_weight], axis=1),
    )
    cols = embeds.reshape(resp_dev, n_zl, n_plane, rows_w).transpose(2, 0, 1, 3)
    cols = lax.all_to_all(cols, PLANE, 0, 0, tiled=True).reshape(n_plane * resp_dev, n_zl * rows_w)
    part = jnp.concatenate(
        [
            jnp.dot(cols, pair_w[0], preferred_element_type=jnp.float32),
            jnp.dot(cols, pair_w[1], preferred_element_type=jnp.float32),
        ],
        axis=1,
    )
    part = part.reshape(n_plane, resp_dev, part.shape[1])
    proj = jnp.sum(lax.all_to_all(part, PLANE, 0, 0, tiled=True), axis=0)

    base = (jnp.arange(prompts_dev, dtype=jnp.int32) * groups)[:, None]
    row_a = base + jnp.take_along_axis(owner, pairs[:, :, 0], axis=1)
    row_b = base + jnp.take_along_axis(owner, pairs[:, :, 1], axis=1)
    upper = proj[:, :width_local][row_a.reshape(-1)]
    lower = proj[:, width_local:][row_b.reshape(-1)]
    pre = (upper + lower).reshape(prompts_dev, npairs, width_local)
    hidden = jax.nn.gelu(pre + pref_bias)
    partial_logit = jnp.sum(hidden * pref_out, axis=-1)
    logit = lax.psum(partial_logit, TP)
    prob = jax.nn.sigmoid(logit)
    numbers = jnp.arange(groups, dtype=jnp.int32)
    first = (pairs[:, :, 0][:, :, None] == numbers).astype(jnp.float32)
    second = (pairs[:, :, 1][:, :, None] == numbers).astype(jnp.float32)
    wins = jnp.sum(prob[:, :, None] * first + (1.0 - prob)[:, :, None] * second, axis=1)
    count = jnp.sum(first + second, axis=1)
    winrate = (wins + 1.0) / (count + 2.0)
    placed = (owner[:, :, None] == numbers).astype(jnp.float32)
    rowrate = jnp.sum(winrate[:, :, None] * placed, axis=1).reshape(-1)
    coef = 2.0 * (logratio - eta_scale * (rowrate - 0.5))
    weighted = (
        (
            features.astype(jnp.float32).reshape(resp_dev, -1, features.shape[1])
            * coef[:, None, None]
        )
        .reshape(features.shape)
        .astype(jnp.bfloat16)
    )
    total_resp = resp_dev * n_dp
    full = lax.dot_general(
        weighted, attn_out, (((0,), (0,)), ((), ())), preferred_element_type=jnp.float32
    )
    full = full.astype(jnp.bfloat16).reshape(n_zl, n_plane, -1, full.shape[1])
    shares = lax.all_to_all(full.transpose(1, 0, 2, 3), PLANE, 0, 0, tiled=True)
    plane_sum = jnp.sum(shares.astype(jnp.float32), axis=0)
    mine = jnp.where(zl == 0, plane_sum[0], plane_sum[1])
    theirs = jnp.where(zl == 0, plane_sum[1], plane_sum[0])
    d_attn = jnp.dot(weighted, piece, preferred_element_type=jnp.float32).astype(jnp.bfloat16)
    o_grad = (mine + lax.ppermute(theirs, "zl", swap)) / total_resp
    return (d_attn, o_grad)


def solution(mesh):
    n_zl = 2
    fine = Mesh(
        mesh.devices.reshape(
            n_zl, mesh.shape["dp"] // (n_zl * 4), 4, mesh.shape["tensor"] // 2, 2
        ),
        ("zl", "y", "x", "zh", "c"),
    )
    return jax.shard_map(
        shards,
        mesh=fine,
        in_specs=(
            P(DP, None),
            P(DP, None),
            P(DP, None, None),
            P(None, DP, TP),
            P(TP),
            P(TP),
            P(DP),
            P(DP, TP),
            P(DP, TP),
            P(DP, TP),
        ),
        out_specs=(P(DP, TP), P(DP, TP)),
        check_vma=False,
    )
```

```python
import jax
import jax.numpy as jnp
from jax import lax
from jax.sharding import Mesh
from jax.sharding import PartitionSpec as P

eta_scale = 2.0

DP = ("zl", "y", "x")
TP = ("zh", "c")
PLANE = ("y", "x")


def shards(
    embeds, owner, pairs, pref_weight, pref_bias, pref_out, logratio, attn_out, grad_out, w_out
):
    resp_dev = embeds.shape[0]
    prompts_dev = owner.shape[0]
    groups = owner.shape[1]
    npairs = pairs.shape[1]
    width_local = pref_weight.shape[2]
    rows_w = pref_weight.shape[1]
    n_dp = lax.axis_size(DP)
    n_zl = lax.axis_size("zl")
    n_plane = lax.axis_size(PLANE)
    zl = lax.axis_index("zl")
    swap = [(k, (k + 1) % n_zl) for k in range(n_zl)]
    w_other = lax.ppermute(w_out, "zl", swap)
    other = lax.ppermute(pref_weight, "zl", swap)
    grad_out, w_other, other = lax.optimization_barrier((grad_out, w_other, other))
    features = lax.all_gather(grad_out, TP, axis=1, tiled=True)
    w_pair = jnp.where(zl == 0, jnp.stack([w_out, w_other]), jnp.stack([w_other, w_out]))
    copies = jnp.broadcast_to(w_pair[None], (n_plane,) + w_pair.shape)
    piece = lax.all_to_all(copies, PLANE, 0, 0, tiled=True)
    piece = piece.transpose(1, 0, 2, 3).reshape(-1, w_out.shape[1])

    pair_w = jnp.where(
        zl == 0,
        jnp.concatenate([pref_weight, other], axis=1),
        jnp.concatenate([other, pref_weight], axis=1),
    )
    cols = embeds.reshape(resp_dev, n_zl, n_plane, rows_w).transpose(2, 0, 1, 3)
    cols = lax.all_to_all(cols, PLANE, 0, 0, tiled=True).reshape(n_plane * resp_dev, n_zl * rows_w)
    part = jnp.concatenate(
        [
            jnp.dot(cols, pair_w[0], preferred_element_type=jnp.float32),
            jnp.dot(cols, pair_w[1], preferred_element_type=jnp.float32),
        ],
        axis=1,
    )
    part = part.reshape(n_plane, resp_dev, part.shape[1])
    proj = jnp.sum(lax.all_to_all(part, PLANE, 0, 0, tiled=True), axis=0)

    base = (jnp.arange(prompts_dev, dtype=jnp.int32) * groups)[:, None]
    row_a = base + jnp.take_along_axis(owner, pairs[:, :, 0], axis=1)
    row_b = base + jnp.take_along_axis(owner, pairs[:, :, 1], axis=1)
    upper = proj[:, :width_local][row_a.reshape(-1)]
    lower = proj[:, width_local:][row_b.reshape(-1)]
    pre = (upper + lower).reshape(prompts_dev, npairs, width_local)
    hidden = jax.nn.gelu(pre + pref_bias)
    partial_logit = jnp.sum(hidden * pref_out, axis=-1)
    logit = lax.psum(partial_logit, TP)
    prob = jax.nn.sigmoid(logit)
    numbers = jnp.arange(groups, dtype=jnp.int32)
    first = (pairs[:, :, 0][:, :, None] == numbers).astype(jnp.float32)
    second = (pairs[:, :, 1][:, :, None] == numbers).astype(jnp.float32)
    wins = jnp.sum(prob[:, :, None] * first + (1.0 - prob)[:, :, None] * second, axis=1)
    count = jnp.sum(first + second, axis=1)
    winrate = (wins + 1.0) / (count + 2.0)
    placed = (owner[:, :, None] == numbers).astype(jnp.float32)
    rowrate = jnp.sum(winrate[:, :, None] * placed, axis=1).reshape(-1)
    coef = 2.0 * (logratio - eta_scale * (rowrate - 0.5))
    weighted = (
        (
            features.astype(jnp.float32).reshape(resp_dev, -1, features.shape[1])
            * coef[:, None, None]
        )
        .reshape(features.shape)
        .astype(jnp.bfloat16)
    )
    total_resp = resp_dev * n_dp
    full = lax.dot_general(
        weighted, attn_out, (((0,), (0,)), ((), ())), preferred_element_type=jnp.float32
    )
    full = full.astype(jnp.bfloat16).reshape(n_zl, n_plane, -1, full.shape[1])
    shares = lax.all_to_all(full.transpose(1, 0, 2, 3), PLANE, 0, 0, tiled=True)
    plane_sum = jnp.sum(shares.astype(jnp.float32), axis=0)
    mine = jnp.where(zl == 0, plane_sum[0], plane_sum[1])
    theirs = jnp.where(zl == 0, plane_sum[1], plane_sum[0])
    d_attn = jnp.dot(weighted, piece, preferred_element_type=jnp.float32).astype(jnp.bfloat16)
    o_grad = (mine + lax.ppermute(theirs, "zl", swap)) / total_resp
    return (d_attn, o_grad)


def solution(mesh):
    n_zl = 2
    fine = Mesh(
        mesh.devices.reshape(
            n_zl, mesh.shape["dp"] // (n_zl * 4), 4, mesh.shape["tensor"] // 2, 2
        ),
        ("zl", "y", "x", "zh", "c"),
    )
    return jax.shard_map(
        shards,
        mesh=fine,
        in_specs=(
            P(DP, None),
            P(DP, None),
            P(DP, None, None),
            P(None, DP, TP),
            P(TP),
            P(TP),
            P(DP),
            P(DP, TP),
            P(DP, TP),
            P(DP, TP),
        ),
        out_specs=(P(DP, TP), P(DP, TP)),
        check_vma=False,
    )
```

```python
import jax
import jax.numpy as jnp
from jax import lax
from jax.sharding import Mesh
from jax.sharding import PartitionSpec as P

eta_scale = 2.0

DP = ("zl", "y", "x")
TP = ("zh", "c")
PLANE = ("y", "x")


def shards(
    embeds, owner, pairs, pref_weight, pref_bias, pref_out, logratio, attn_out, grad_out, w_out
):
    resp_dev = embeds.shape[0]
    prompts_dev = owner.shape[0]
    groups = owner.shape[1]
    npairs = pairs.shape[1]
    width_local = pref_weight.shape[2]
    rows_w = pref_weight.shape[1]
    n_dp = lax.axis_size(DP)
    n_zl = lax.axis_size("zl")
    n_plane = lax.axis_size(PLANE)
    zl = lax.axis_index("zl")
    swap = [(k, (k + 1) % n_zl) for k in range(n_zl)]
    w_other = lax.ppermute(w_out, "zl", swap)
    other = lax.ppermute(pref_weight, "zl", swap)
    grad_out, w_other, other = lax.optimization_barrier((grad_out, w_other, other))
    features = lax.all_gather(grad_out, TP, axis=1, tiled=True)
    w_pair = jnp.where(zl == 0, jnp.stack([w_out, w_other]), jnp.stack([w_other, w_out]))
    copies = jnp.broadcast_to(w_pair[None], (n_plane,) + w_pair.shape)
    piece = lax.all_to_all(copies, PLANE, 0, 0, tiled=True)
    piece = piece.transpose(1, 0, 2, 3).reshape(-1, w_out.shape[1])

    pair_w = jnp.where(
        zl == 0,
        jnp.concatenate([pref_weight, other], axis=1),
        jnp.concatenate([other, pref_weight], axis=1),
    )
    cols = embeds.reshape(resp_dev, n_zl, n_plane, rows_w).transpose(2, 0, 1, 3)
    cols = lax.all_to_all(cols, PLANE, 0, 0, tiled=True).reshape(n_plane * resp_dev, n_zl * rows_w)
    part = jnp.concatenate(
        [
            jnp.dot(cols, pair_w[0], preferred_element_type=jnp.float32),
            jnp.dot(cols, pair_w[1], preferred_element_type=jnp.float32),
        ],
        axis=1,
    )
    part = part.reshape(n_plane, resp_dev, part.shape[1])
    proj = jnp.sum(lax.all_to_all(part, PLANE, 0, 0, tiled=True), axis=0)

    base = (jnp.arange(prompts_dev, dtype=jnp.int32) * groups)[:, None]
    row_a = base + jnp.take_along_axis(owner, pairs[:, :, 0], axis=1)
    row_b = base + jnp.take_along_axis(owner, pairs[:, :, 1], axis=1)
    upper = proj[:, :width_local][row_a.reshape(-1)]
    lower = proj[:, width_local:][row_b.reshape(-1)]
    pre = (upper + lower).reshape(prompts_dev, npairs, width_local)
    hidden = jax.nn.gelu(pre + pref_bias)
    partial_logit = jnp.sum(hidden * pref_out, axis=-1)
    logit = lax.psum(partial_logit, TP)
    prob = jax.nn.sigmoid(logit)
    numbers = jnp.arange(groups, dtype=jnp.int32)
    first = (pairs[:, :, 0][:, :, None] == numbers).astype(jnp.float32)
    second = (pairs[:, :, 1][:, :, None] == numbers).astype(jnp.float32)
    wins = jnp.sum(prob[:, :, None] * first + (1.0 - prob)[:, :, None] * second, axis=1)
    count = jnp.sum(first + second, axis=1)
    winrate = (wins + 1.0) / (count + 2.0)
    placed = (owner[:, :, None] == numbers).astype(jnp.float32)
    rowrate = jnp.sum(winrate[:, :, None] * placed, axis=1).reshape(-1)
    coef = 2.0 * (logratio - eta_scale * (rowrate - 0.5))
    weighted = (
        (
            features.astype(jnp.float32).reshape(resp_dev, -1, features.shape[1])
            * coef[:, None, None]
        )
        .reshape(features.shape)
        .astype(jnp.bfloat16)
    )
    total_resp = resp_dev * n_dp
    full = lax.dot_general(
        weighted, attn_out, (((0,), (0,)), ((), ())), preferred_element_type=jnp.float32
    )
    full = full.astype(jnp.bfloat16).reshape(n_zl, n_plane, -1, full.shape[1])
    shares = lax.all_to_all(full.transpose(1, 0, 2, 3), PLANE, 0, 0, tiled=True)
    d_attn = jnp.dot(weighted, piece, preferred_element_type=jnp.float32).astype(jnp.bfloat16)
    shares, d_attn = lax.optimization_barrier((shares, d_attn))
    plane_sum = jnp.sum(shares.astype(jnp.float32), axis=0)
    mine = jnp.where(zl == 0, plane_sum[0], plane_sum[1])
    theirs = jnp.where(zl == 0, plane_sum[1], plane_sum[0])
    o_grad = (mine + lax.ppermute(theirs, "zl", swap)) / total_resp
    return (d_attn, o_grad)


def solution(mesh):
    n_zl = 2
    fine = Mesh(
        mesh.devices.reshape(
            n_zl, mesh.shape["dp"] // (n_zl * 4), 4, mesh.shape["tensor"] // 2, 2
        ),
        ("zl", "y", "x", "zh", "c"),
    )
    return jax.shard_map(
        shards,
        mesh=fine,
        in_specs=(
            P(DP, None),
            P(DP, None),
            P(DP, None, None),
            P(None, DP, TP),
            P(TP),
            P(TP),
            P(DP),
            P(DP, TP),
            P(DP, TP),
            P(DP, TP),
        ),
        out_specs=(P(DP, TP), P(DP, TP)),
        check_vma=False,
    )
```

```python
import jax
import jax.numpy as jnp
from jax import lax
from jax.sharding import Mesh
from jax.sharding import PartitionSpec as P

eta_scale = 2.0

DP = ("zl", "y", "x")
TP = ("zh", "c")
PLANE = ("y", "x")


def shards(
    embeds, owner, pairs, pref_weight, pref_bias, pref_out, logratio, attn_out, grad_out, w_out
):
    resp_dev = embeds.shape[0]
    prompts_dev = owner.shape[0]
    groups = owner.shape[1]
    npairs = pairs.shape[1]
    width_local = pref_weight.shape[2]
    rows_w = pref_weight.shape[1]
    n_dp = lax.axis_size(DP)
    n_zl = lax.axis_size("zl")
    n_plane = lax.axis_size(PLANE)
    zl = lax.axis_index("zl")
    swap = [(k, (k + 1) % n_zl) for k in range(n_zl)]
    w_other = lax.ppermute(w_out, "zl", swap)
    other = lax.ppermute(pref_weight, "zl", swap)
    grad_out, w_other, other = lax.optimization_barrier((grad_out, w_other, other))
    features = lax.all_gather(grad_out, TP, axis=1, tiled=True)
    w_pair = jnp.where(zl == 0, jnp.stack([w_out, w_other]), jnp.stack([w_other, w_out]))
    copies = jnp.broadcast_to(w_pair[None], (n_plane,) + w_pair.shape)
    piece = lax.all_to_all(copies, PLANE, 0, 0, tiled=True)
    piece = piece.transpose(1, 0, 2, 3).reshape(-1, w_out.shape[1])

    pair_w = jnp.where(
        zl == 0,
        jnp.concatenate([pref_weight, other], axis=1),
        jnp.concatenate([other, pref_weight], axis=1),
    )
    cols = embeds.reshape(resp_dev, n_zl, n_plane, rows_w).transpose(2, 0, 1, 3)
    cols = lax.all_to_all(cols, PLANE, 0, 0, tiled=True).reshape(n_plane * resp_dev, n_zl * rows_w)
    part = jnp.concatenate(
        [
            jnp.dot(cols, pair_w[0], preferred_element_type=jnp.float32),
            jnp.dot(cols, pair_w[1], preferred_element_type=jnp.float32),
        ],
        axis=1,
    )
    part = part.reshape(n_plane, resp_dev, part.shape[1])
    proj = jnp.sum(lax.all_to_all(part, PLANE, 0, 0, tiled=True), axis=0)

    base = (jnp.arange(prompts_dev, dtype=jnp.int32) * groups)[:, None]
    row_a = base + jnp.take_along_axis(owner, pairs[:, :, 0], axis=1)
    row_b = base + jnp.take_along_axis(owner, pairs[:, :, 1], axis=1)
    upper = proj[:, :width_local][row_a.reshape(-1)]
    lower = proj[:, width_local:][row_b.reshape(-1)]
    pre = (upper + lower).reshape(prompts_dev, npairs, width_local)
    hidden = jax.nn.gelu(pre + pref_bias)
    partial_logit = jnp.sum(hidden * pref_out, axis=-1)
    logit = lax.psum(partial_logit, TP)
    prob = jax.nn.sigmoid(logit)
    numbers = jnp.arange(groups, dtype=jnp.int32)
    first = (pairs[:, :, 0][:, :, None] == numbers).astype(jnp.float32)
    second = (pairs[:, :, 1][:, :, None] == numbers).astype(jnp.float32)
    wins = jnp.sum(prob[:, :, None] * first + (1.0 - prob)[:, :, None] * second, axis=1)
    count = jnp.sum(first + second, axis=1)
    winrate = (wins + 1.0) / (count + 2.0)
    placed = (owner[:, :, None] == numbers).astype(jnp.float32)
    rowrate = jnp.sum(winrate[:, :, None] * placed, axis=1).reshape(-1)
    coef = 2.0 * (logratio - eta_scale * (rowrate - 0.5))
    weighted = (
        (
            features.astype(jnp.float32).reshape(resp_dev, -1, features.shape[1])
            * coef[:, None, None]
        )
        .reshape(features.shape)
        .astype(jnp.bfloat16)
    )
    total_resp = resp_dev * n_dp
    full = lax.dot_general(
        weighted, attn_out, (((0,), (0,)), ((), ())), preferred_element_type=jnp.float32
    )
    full = full.astype(jnp.bfloat16).reshape(n_zl, n_plane, -1, full.shape[1])
    first_half = jnp.where(zl == 0, full[1], full[0])
    own_half = jnp.where(zl == 0, full[0], full[1])
    theirs = jnp.sum(lax.all_to_all(first_half, PLANE, 0, 0, tiled=True).astype(jnp.float32), axis=0)
    got = lax.ppermute(theirs, "zl", swap)
    shares = lax.all_to_all(own_half, PLANE, 0, 0, tiled=True)
    d_attn = jnp.dot(weighted, piece, preferred_element_type=jnp.float32).astype(jnp.bfloat16)
    shares, d_attn = lax.optimization_barrier((shares, d_attn))
    mine = jnp.sum(shares.astype(jnp.float32), axis=0)
    o_grad = (mine + got) / total_resp
    return (d_attn, o_grad)


def solution(mesh):
    n_zl = 2
    fine = Mesh(
        mesh.devices.reshape(
            n_zl, mesh.shape["dp"] // (n_zl * 4), 4, mesh.shape["tensor"] // 2, 2
        ),
        ("zl", "y", "x", "zh", "c"),
    )
    return jax.shard_map(
        shards,
        mesh=fine,
        in_specs=(
            P(DP, None),
            P(DP, None),
            P(DP, None, None),
            P(None, DP, TP),
            P(TP),
            P(TP),
            P(DP),
            P(DP, TP),
            P(DP, TP),
            P(DP, TP),
        ),
        out_specs=(P(DP, TP), P(DP, TP)),
        check_vma=False,
    )
```

```python
import jax
import jax.numpy as jnp
from jax import lax
from jax.sharding import Mesh
from jax.sharding import PartitionSpec as P

eta_scale = 2.0


DP = ("zl", "y", "x")
TP = ("zh", "c")
PLANE = ("y", "x")


def shards(
    embeds, owner, pairs, pref_weight, pref_bias, pref_out, logratio, attn_out, grad_out, w_out
):
    resp_dev = embeds.shape[0]
    prompts_dev = owner.shape[0]
    groups = owner.shape[1]
    npairs = pairs.shape[1]
    width_local = pref_weight.shape[2]
    rows_w = pref_weight.shape[1]
    n_dp = lax.axis_size(DP)
    n_zl = lax.axis_size("zl")
    n_plane = lax.axis_size(PLANE)
    zl = lax.axis_index("zl")
    swap = [(k, (k + 1) % n_zl) for k in range(n_zl)]
    w_other = lax.ppermute(w_out, "zl", swap)
    other = lax.ppermute(pref_weight, "zl", swap)
    grad_out, w_other, other = lax.optimization_barrier((grad_out, w_other, other))
    features = lax.all_gather(grad_out, TP, axis=1, tiled=True)
    w_pair = jnp.where(zl == 0, jnp.stack([w_out, w_other]), jnp.stack([w_other, w_out]))
    n_y = lax.axis_size("y")
    n_x = lax.axis_size("x")
    y = lax.axis_index("y")
    x = lax.axis_index("x")
    got = [w_pair]
    for dy in range(n_y):
        for dx in range(n_x):
            if dy == 0 and dx == 0:
                continue
            perm = [
                (a * n_x + b, ((a + dy) % n_y) * n_x + (b + dx) % n_x)
                for a in range(n_y)
                for b in range(n_x)
            ]
            got.append(lax.ppermute(w_pair, PLANE, perm))
    sy = jnp.arange(n_y * n_x, dtype=jnp.int32) // n_x
    sx = jnp.arange(n_y * n_x, dtype=jnp.int32) % n_x
    shift = ((y - sy) % n_y) * n_x + (x - sx) % n_x
    blocks = jnp.take(jnp.stack(got), shift, axis=0)
    piece = blocks.transpose(1, 0, 2, 3).reshape(-1, w_out.shape[1])

    pair_w = jnp.where(
        zl == 0,
        jnp.concatenate([pref_weight, other], axis=1),
        jnp.concatenate([other, pref_weight], axis=1),
    )
    cols = embeds.reshape(resp_dev, n_zl, n_plane, rows_w).transpose(2, 0, 1, 3)
    cols = lax.all_to_all(cols, PLANE, 0, 0, tiled=True).reshape(n_plane * resp_dev, n_zl * rows_w)
    part = jnp.concatenate(
        [
            jnp.dot(cols, pair_w[0], preferred_element_type=jnp.float32),
            jnp.dot(cols, pair_w[1], preferred_element_type=jnp.float32),
        ],
        axis=1,
    )
    part = part.reshape(n_plane, resp_dev, part.shape[1])
    proj = jnp.sum(lax.all_to_all(part, PLANE, 0, 0, tiled=True), axis=0)

    base = (jnp.arange(prompts_dev, dtype=jnp.int32) * groups)[:, None]
    row_a = base + jnp.take_along_axis(owner, pairs[:, :, 0], axis=1)
    row_b = base + jnp.take_along_axis(owner, pairs[:, :, 1], axis=1)
    upper = proj[:, :width_local][row_a.reshape(-1)]
    lower = proj[:, width_local:][row_b.reshape(-1)]
    pre = (upper + lower).reshape(prompts_dev, npairs, width_local)
    hidden = jax.nn.gelu(pre + pref_bias)
    partial_logit = jnp.sum(hidden * pref_out, axis=-1)
    logit = lax.psum(partial_logit, TP)
    prob = jax.nn.sigmoid(logit)
    numbers = jnp.arange(groups, dtype=jnp.int32)
    first = (pairs[:, :, 0][:, :, None] == numbers).astype(jnp.float32)
    second = (pairs[:, :, 1][:, :, None] == numbers).astype(jnp.float32)
    wins = jnp.sum(prob[:, :, None] * first + (1.0 - prob)[:, :, None] * second, axis=1)
    count = jnp.sum(first + second, axis=1)
    winrate = (wins + 1.0) / (count + 2.0)
    placed = (owner[:, :, None] == numbers).astype(jnp.float32)
    rowrate = jnp.sum(winrate[:, :, None] * placed, axis=1).reshape(-1)
    coef = 2.0 * (logratio - eta_scale * (rowrate - 0.5))
    weighted = (
        (
            features.astype(jnp.float32).reshape(resp_dev, -1, features.shape[1])
            * coef[:, None, None]
        )
        .reshape(features.shape)
        .astype(jnp.bfloat16)
    )
    total_resp = resp_dev * n_dp
    full = lax.dot_general(
        weighted, attn_out, (((0,), (0,)), ((), ())), preferred_element_type=jnp.float32
    )
    full = full.astype(jnp.bfloat16).reshape(n_zl, n_plane, -1, full.shape[1])
    first_half = jnp.where(zl == 0, full[1], full[0])
    own_half = jnp.where(zl == 0, full[0], full[1])
    theirs = jnp.sum(lax.all_to_all(first_half, PLANE, 0, 0, tiled=True).astype(jnp.float32), axis=0)
    got = lax.ppermute(theirs, "zl", swap)
    shares = lax.all_to_all(own_half, PLANE, 0, 0, tiled=True)
    d_attn = jnp.dot(weighted, piece, preferred_element_type=jnp.float32).astype(jnp.bfloat16)
    shares, d_attn = lax.optimization_barrier((shares, d_attn))
    mine = jnp.sum(shares.astype(jnp.float32), axis=0)
    o_grad = (mine + got) / total_resp
    return (d_attn, o_grad)


def solution(mesh):
    n_zl = 2
    fine = Mesh(
        mesh.devices.reshape(
            n_zl, mesh.shape["dp"] // (n_zl * 4), 4, mesh.shape["tensor"] // 2, 2
        ),
        ("zl", "y", "x", "zh", "c"),
    )
    return jax.shard_map(
        shards,
        mesh=fine,
        in_specs=(
            P(DP, None),
            P(DP, None),
            P(DP, None, None),
            P(None, DP, TP),
            P(TP),
            P(TP),
            P(DP),
            P(DP, TP),
            P(DP, TP),
            P(DP, TP),
        ),
        out_specs=(P(DP, TP), P(DP, TP)),
        check_vma=False,
    )
```

```python
import jax
import jax.numpy as jnp
from jax import lax
from jax.sharding import Mesh
from jax.sharding import PartitionSpec as P

eta_scale = 2.0

DP = ("zl", "y", "x")
TP = ("zh", "c")
PLANE = ("y", "x")


def shards(
    embeds, owner, pairs, pref_weight, pref_bias, pref_out, logratio, attn_out, grad_out, w_out
):
    resp_dev = embeds.shape[0]
    prompts_dev = owner.shape[0]
    groups = owner.shape[1]
    npairs = pairs.shape[1]
    width_local = pref_weight.shape[2]
    rows_w = pref_weight.shape[1]
    n_dp = lax.axis_size(DP)
    n_zl = lax.axis_size("zl")
    n_plane = lax.axis_size(PLANE)
    zl = lax.axis_index("zl")
    swap = [(k, (k + 1) % n_zl) for k in range(n_zl)]
    features = lax.all_gather(grad_out, TP, axis=1, tiled=True)
    w_other = lax.ppermute(w_out, "zl", swap)
    other = lax.ppermute(pref_weight, "zl", swap)
    w_pair = jnp.where(zl == 0, jnp.stack([w_out, w_other]), jnp.stack([w_other, w_out]))
    copies = jnp.broadcast_to(w_pair[None], (n_plane,) + w_pair.shape)
    piece = lax.all_to_all(copies, PLANE, 0, 0, tiled=True)
    piece = piece.transpose(1, 0, 2, 3).reshape(-1, w_out.shape[1])

    pair_w = jnp.where(
        zl == 0,
        jnp.concatenate([pref_weight, other], axis=1),
        jnp.concatenate([other, pref_weight], axis=1),
    )
    cols = embeds.reshape(resp_dev, n_zl, n_plane, rows_w).transpose(2, 0, 1, 3)
    cols = lax.all_to_all(cols, PLANE, 0, 0, tiled=True).reshape(n_plane * resp_dev, n_zl * rows_w)
    part = jnp.concatenate(
        [
            jnp.dot(cols, pair_w[0], preferred_element_type=jnp.float32),
            jnp.dot(cols, pair_w[1], preferred_element_type=jnp.float32),
        ],
        axis=1,
    )
    part = part.reshape(n_plane, resp_dev, part.shape[1])
    proj = jnp.sum(lax.all_to_all(part, PLANE, 0, 0, tiled=True), axis=0)

    base = (jnp.arange(prompts_dev, dtype=jnp.int32) * groups)[:, None]
    row_a = base + jnp.take_along_axis(owner, pairs[:, :, 0], axis=1)
    row_b = base + jnp.take_along_axis(owner, pairs[:, :, 1], axis=1)
    upper = proj[:, :width_local][row_a.reshape(-1)]
    lower = proj[:, width_local:][row_b.reshape(-1)]
    pre = (upper + lower).reshape(prompts_dev, npairs, width_local)
    hidden = jax.nn.gelu(pre + pref_bias)
    partial_logit = jnp.sum(hidden * pref_out, axis=-1)
    logit = lax.psum(partial_logit, TP)
    prob = jax.nn.sigmoid(logit)
    numbers = jnp.arange(groups, dtype=jnp.int32)
    first = (pairs[:, :, 0][:, :, None] == numbers).astype(jnp.float32)
    second = (pairs[:, :, 1][:, :, None] == numbers).astype(jnp.float32)
    wins = jnp.sum(prob[:, :, None] * first + (1.0 - prob)[:, :, None] * second, axis=1)
    count = jnp.sum(first + second, axis=1)
    winrate = (wins + 1.0) / (count + 2.0)
    placed = (owner[:, :, None] == numbers).astype(jnp.float32)
    rowrate = jnp.sum(winrate[:, :, None] * placed, axis=1).reshape(-1)
    coef = 2.0 * (logratio - eta_scale * (rowrate - 0.5))
    weighted = (
        (
            features.astype(jnp.float32).reshape(resp_dev, -1, features.shape[1])
            * coef[:, None, None]
        )
        .reshape(features.shape)
        .astype(jnp.bfloat16)
    )
    total_resp = resp_dev * n_dp
    full = lax.dot_general(
        weighted, attn_out, (((0,), (0,)), ((), ())), preferred_element_type=jnp.float32
    )
    full = full.astype(jnp.bfloat16).reshape(n_zl, n_plane, -1, full.shape[1])
    first_half = jnp.where(zl == 0, full[1], full[0])
    own_half = jnp.where(zl == 0, full[0], full[1])
    theirs = jnp.sum(lax.all_to_all(first_half, PLANE, 0, 0, tiled=True).astype(jnp.float32), axis=0)
    got = lax.ppermute(theirs, "zl", swap)
    shares = lax.all_to_all(own_half, PLANE, 0, 0, tiled=True)
    d_attn = jnp.dot(weighted, piece, preferred_element_type=jnp.float32).astype(jnp.bfloat16)
    shares, d_attn = lax.optimization_barrier((shares, d_attn))
    mine = jnp.sum(shares.astype(jnp.float32), axis=0)
    o_grad = (mine + got) / total_resp
    return (d_attn, o_grad)


def solution(mesh):
    n_zl = 2
    fine = Mesh(
        mesh.devices.reshape(
            n_zl, mesh.shape["dp"] // (n_zl * 4), 4, mesh.shape["tensor"] // 2, 2
        ),
        ("zl", "y", "x", "zh", "c"),
    )
    return jax.shard_map(
        shards,
        mesh=fine,
        in_specs=(
            P(DP, None),
            P(DP, None),
            P(DP, None, None),
            P(None, DP, TP),
            P(TP),
            P(TP),
            P(DP),
            P(DP, TP),
            P(DP, TP),
            P(DP, TP),
        ),
        out_specs=(P(DP, TP), P(DP, TP)),
        check_vma=False,
    )
```

```python
import jax
import jax.numpy as jnp
from jax import lax
from jax.sharding import Mesh
from jax.sharding import PartitionSpec as P

eta_scale = 2.0

DP = ("zl", "y", "x")
TP = ("zh", "c")
PLANE = ("y", "x")


def shards(
    embeds, owner, pairs, pref_weight, pref_bias, pref_out, logratio, attn_out, grad_out, w_out
):
    resp_dev = embeds.shape[0]
    prompts_dev = owner.shape[0]
    groups = owner.shape[1]
    npairs = pairs.shape[1]
    width_local = pref_weight.shape[2]
    rows_w = pref_weight.shape[1]
    n_dp = lax.axis_size(DP)
    n_zl = lax.axis_size("zl")
    n_plane = lax.axis_size(PLANE)
    zl = lax.axis_index("zl")
    swap = [(k, (k + 1) % n_zl) for k in range(n_zl)]
    features = lax.all_gather(grad_out, TP, axis=1, tiled=True)
    other = lax.ppermute(pref_weight, "zl", swap)
    copies = jnp.broadcast_to(w_out[None], (n_plane,) + w_out.shape)
    plane_w = lax.all_to_all(copies, PLANE, 0, 0, tiled=True).reshape(-1, w_out.shape[1])

    pair_w = jnp.where(
        zl == 0,
        jnp.concatenate([pref_weight, other], axis=1),
        jnp.concatenate([other, pref_weight], axis=1),
    )
    cols = embeds.reshape(resp_dev, n_zl, n_plane, rows_w).transpose(2, 0, 1, 3)
    cols = lax.all_to_all(cols, PLANE, 0, 0, tiled=True).reshape(n_plane * resp_dev, n_zl * rows_w)
    part = jnp.concatenate(
        [
            jnp.dot(cols, pair_w[0], preferred_element_type=jnp.float32),
            jnp.dot(cols, pair_w[1], preferred_element_type=jnp.float32),
        ],
        axis=1,
    )
    part = part.reshape(n_plane, resp_dev, part.shape[1])
    proj = jnp.sum(lax.all_to_all(part, PLANE, 0, 0, tiled=True), axis=0)

    base = (jnp.arange(prompts_dev, dtype=jnp.int32) * groups)[:, None]
    row_a = base + jnp.take_along_axis(owner, pairs[:, :, 0], axis=1)
    row_b = base + jnp.take_along_axis(owner, pairs[:, :, 1], axis=1)
    upper = proj[:, :width_local][row_a.reshape(-1)]
    lower = proj[:, width_local:][row_b.reshape(-1)]
    pre = (upper + lower).reshape(prompts_dev, npairs, width_local)
    hidden = jax.nn.gelu(pre + pref_bias)
    partial_logit = jnp.sum(hidden * pref_out, axis=-1)
    logit = lax.psum(partial_logit, TP)
    prob = jax.nn.sigmoid(logit)
    numbers = jnp.arange(groups, dtype=jnp.int32)
    first = (pairs[:, :, 0][:, :, None] == numbers).astype(jnp.float32)
    second = (pairs[:, :, 1][:, :, None] == numbers).astype(jnp.float32)
    wins = jnp.sum(prob[:, :, None] * first + (1.0 - prob)[:, :, None] * second, axis=1)
    count = jnp.sum(first + second, axis=1)
    winrate = (wins + 1.0) / (count + 2.0)
    placed = (owner[:, :, None] == numbers).astype(jnp.float32)
    rowrate = jnp.sum(winrate[:, :, None] * placed, axis=1).reshape(-1)
    coef = 2.0 * (logratio - eta_scale * (rowrate - 0.5))
    weighted = (
        (
            features.astype(jnp.float32).reshape(resp_dev, -1, features.shape[1])
            * coef[:, None, None]
        )
        .reshape(features.shape)
        .astype(jnp.bfloat16)
    )
    total_resp = resp_dev * n_dp
    plane_w, features = lax.optimization_barrier((plane_w, features))
    w_half = lax.ppermute(plane_w, "zl", swap)
    piece = jnp.where(
        zl == 0,
        jnp.concatenate([plane_w, w_half], axis=0),
        jnp.concatenate([w_half, plane_w], axis=0),
    )
    full = lax.dot_general(
        weighted, attn_out, (((0,), (0,)), ((), ())), preferred_element_type=jnp.float32
    )
    full = full.astype(jnp.bfloat16).reshape(n_zl, n_plane, -1, full.shape[1])
    first_half = jnp.where(zl == 0, full[1], full[0])
    own_half = jnp.where(zl == 0, full[0], full[1])
    theirs = jnp.sum(lax.all_to_all(first_half, PLANE, 0, 0, tiled=True).astype(jnp.float32), axis=0)
    got = lax.ppermute(theirs, "zl", swap)
    shares = lax.all_to_all(own_half, PLANE, 0, 0, tiled=True)
    d_attn = jnp.dot(weighted, piece, preferred_element_type=jnp.float32).astype(jnp.bfloat16)
    shares, d_attn = lax.optimization_barrier((shares, d_attn))
    mine = jnp.sum(shares.astype(jnp.float32), axis=0)
    o_grad = (mine + got) / total_resp
    return (d_attn, o_grad)


def solution(mesh):
    n_zl = 2
    fine = Mesh(
        mesh.devices.reshape(
            n_zl, mesh.shape["dp"] // (n_zl * 4), 4, mesh.shape["tensor"] // 2, 2
        ),
        ("zl", "y", "x", "zh", "c"),
    )
    return jax.shard_map(
        shards,
        mesh=fine,
        in_specs=(
            P(DP, None),
            P(DP, None),
            P(DP, None, None),
            P(None, DP, TP),
            P(TP),
            P(TP),
            P(DP),
            P(DP, TP),
            P(DP, TP),
            P(DP, TP),
        ),
        out_specs=(P(DP, TP), P(DP, TP)),
        check_vma=False,
    )
```

```python
import jax
import jax.numpy as jnp
from jax import lax
from jax.sharding import Mesh
from jax.sharding import PartitionSpec as P

eta_scale = 2.0

DP = ("zl", "y", "x")
TP = ("zh", "c")
PLANE = ("y", "x")


def shards(
    embeds, owner, pairs, pref_weight, pref_bias, pref_out, logratio, attn_out, grad_out, w_out
):
    resp_dev = embeds.shape[0]
    prompts_dev = owner.shape[0]
    groups = owner.shape[1]
    npairs = pairs.shape[1]
    width_local = pref_weight.shape[2]
    rows_w = pref_weight.shape[1]
    n_dp = lax.axis_size(DP)
    n_zl = lax.axis_size("zl")
    n_plane = lax.axis_size(PLANE)
    zl = lax.axis_index("zl")
    swap = [(k, (k + 1) % n_zl) for k in range(n_zl)]
    features = lax.all_gather(grad_out, TP, axis=1, tiled=True)
    w_other = lax.ppermute(w_out, "zl", swap)
    other = lax.ppermute(pref_weight, "zl", swap)
    w_pair = jnp.where(zl == 0, jnp.stack([w_out, w_other]), jnp.stack([w_other, w_out]))

    pair_w = jnp.where(
        zl == 0,
        jnp.concatenate([pref_weight, other], axis=1),
        jnp.concatenate([other, pref_weight], axis=1),
    )
    cols = embeds.reshape(resp_dev, n_zl, n_plane, rows_w).transpose(2, 0, 1, 3)
    cols = lax.all_to_all(cols, PLANE, 0, 0, tiled=True).reshape(n_plane * resp_dev, n_zl * rows_w)
    part = jnp.concatenate(
        [
            jnp.dot(cols, pair_w[0], preferred_element_type=jnp.float32),
            jnp.dot(cols, pair_w[1], preferred_element_type=jnp.float32),
        ],
        axis=1,
    )
    part = part.reshape(n_plane, resp_dev, part.shape[1])
    proj = jnp.sum(lax.all_to_all(part, PLANE, 0, 0, tiled=True), axis=0)

    base = (jnp.arange(prompts_dev, dtype=jnp.int32) * groups)[:, None]
    row_a = base + jnp.take_along_axis(owner, pairs[:, :, 0], axis=1)
    row_b = base + jnp.take_along_axis(owner, pairs[:, :, 1], axis=1)
    upper = proj[:, :width_local][row_a.reshape(-1)]
    lower = proj[:, width_local:][row_b.reshape(-1)]
    pre = (upper + lower).reshape(prompts_dev, npairs, width_local)
    hidden = jax.nn.gelu(pre + pref_bias)
    partial_logit = jnp.sum(hidden * pref_out, axis=-1)
    logit = lax.psum(partial_logit, TP)
    w_pair, features, logit = lax.optimization_barrier((w_pair, features, logit))
    piece = lax.all_gather(w_pair, PLANE, axis=0, tiled=False)
    piece = piece.transpose(1, 0, 2, 3).reshape(-1, w_out.shape[1])
    prob = jax.nn.sigmoid(logit)
    numbers = jnp.arange(groups, dtype=jnp.int32)
    first = (pairs[:, :, 0][:, :, None] == numbers).astype(jnp.float32)
    second = (pairs[:, :, 1][:, :, None] == numbers).astype(jnp.float32)
    wins = jnp.sum(prob[:, :, None] * first + (1.0 - prob)[:, :, None] * second, axis=1)
    count = jnp.sum(first + second, axis=1)
    winrate = (wins + 1.0) / (count + 2.0)
    placed = (owner[:, :, None] == numbers).astype(jnp.float32)
    rowrate = jnp.sum(winrate[:, :, None] * placed, axis=1).reshape(-1)
    coef = 2.0 * (logratio - eta_scale * (rowrate - 0.5))
    weighted = (
        (
            features.astype(jnp.float32).reshape(resp_dev, -1, features.shape[1])
            * coef[:, None, None]
        )
        .reshape(features.shape)
        .astype(jnp.bfloat16)
    )
    total_resp = resp_dev * n_dp
    full = lax.dot_general(
        weighted, attn_out, (((0,), (0,)), ((), ())), preferred_element_type=jnp.float32
    )
    full = full.astype(jnp.bfloat16).reshape(n_zl, n_plane, -1, full.shape[1])
    first_half = jnp.where(zl == 0, full[1], full[0])
    own_half = jnp.where(zl == 0, full[0], full[1])
    theirs = jnp.sum(lax.all_to_all(first_half, PLANE, 0, 0, tiled=True).astype(jnp.float32), axis=0)
    got = lax.ppermute(theirs, "zl", swap)
    shares = lax.all_to_all(own_half, PLANE, 0, 0, tiled=True)
    d_attn = jnp.dot(weighted, piece, preferred_element_type=jnp.float32).astype(jnp.bfloat16)
    shares, d_attn = lax.optimization_barrier((shares, d_attn))
    mine = jnp.sum(shares.astype(jnp.float32), axis=0)
    o_grad = (mine + got) / total_resp
    return (d_attn, o_grad)


def solution(mesh):
    n_zl = 2
    fine = Mesh(
        mesh.devices.reshape(
            n_zl, mesh.shape["dp"] // (n_zl * 4), 4, mesh.shape["tensor"] // 2, 2
        ),
        ("zl", "y", "x", "zh", "c"),
    )
    return jax.shard_map(
        shards,
        mesh=fine,
        in_specs=(
            P(DP, None),
            P(DP, None),
            P(DP, None, None),
            P(None, DP, TP),
            P(TP),
            P(TP),
            P(DP),
            P(DP, TP),
            P(DP, TP),
            P(DP, TP),
        ),
        out_specs=(P(DP, TP), P(DP, TP)),
        check_vma=False,
    )
```

```python
import jax
import jax.numpy as jnp
from jax import lax
from jax.sharding import Mesh
from jax.sharding import PartitionSpec as P

eta_scale = 2.0

DP = ("zl", "y", "x")
TP = ("zh", "c")
PLANE = ("y", "x")


def shards(
    embeds, owner, pairs, pref_weight, pref_bias, pref_out, logratio, attn_out, grad_out, w_out
):
    resp_dev = embeds.shape[0]
    prompts_dev = owner.shape[0]
    groups = owner.shape[1]
    npairs = pairs.shape[1]
    width_local = pref_weight.shape[2]
    rows_w = pref_weight.shape[1]
    n_dp = lax.axis_size(DP)
    n_zl = lax.axis_size("zl")
    n_plane = lax.axis_size(PLANE)
    zl = lax.axis_index("zl")
    swap = [(k, (k + 1) % n_zl) for k in range(n_zl)]
    features = lax.all_gather(grad_out, TP, axis=1, tiled=True)
    w_other = lax.ppermute(w_out, "zl", swap)
    other = lax.ppermute(pref_weight, "zl", swap)
    w_pair = jnp.where(zl == 0, jnp.stack([w_out, w_other]), jnp.stack([w_other, w_out]))
    copies = jnp.broadcast_to(w_pair[None], (n_plane,) + w_pair.shape)
    piece = lax.all_to_all(copies, PLANE, 0, 0, tiled=True)
    piece = piece.transpose(1, 0, 2, 3).reshape(-1, w_out.shape[1])

    pair_w = jnp.where(
        zl == 0,
        jnp.concatenate([pref_weight, other], axis=1),
        jnp.concatenate([other, pref_weight], axis=1),
    )
    cols = embeds.reshape(resp_dev, n_zl, n_plane, rows_w).transpose(2, 0, 1, 3)
    cols = cols.reshape(n_plane, resp_dev * n_zl * rows_w // 128, 128)
    cols = lax.all_to_all(cols, PLANE, 0, 0, tiled=True).reshape(n_plane * resp_dev, n_zl * rows_w)
    part = jnp.concatenate(
        [
            jnp.dot(cols, pair_w[0], preferred_element_type=jnp.float32),
            jnp.dot(cols, pair_w[1], preferred_element_type=jnp.float32),
        ],
        axis=1,
    )
    part = part.reshape(n_plane, resp_dev, part.shape[1])
    proj = jnp.sum(lax.all_to_all(part, PLANE, 0, 0, tiled=True), axis=0)

    base = (jnp.arange(prompts_dev, dtype=jnp.int32) * groups)[:, None]
    row_a = base + jnp.take_along_axis(owner, pairs[:, :, 0], axis=1)
    row_b = base + jnp.take_along_axis(owner, pairs[:, :, 1], axis=1)
    upper = proj[:, :width_local][row_a.reshape(-1)]
    lower = proj[:, width_local:][row_b.reshape(-1)]
    pre = (upper + lower).reshape(prompts_dev, npairs, width_local)
    hidden = jax.nn.gelu(pre + pref_bias)
    partial_logit = jnp.sum(hidden * pref_out, axis=-1)
    logit = lax.psum(partial_logit, TP)
    prob = jax.nn.sigmoid(logit)
    numbers = jnp.arange(groups, dtype=jnp.int32)
    first = (pairs[:, :, 0][:, :, None] == numbers).astype(jnp.float32)
    second = (pairs[:, :, 1][:, :, None] == numbers).astype(jnp.float32)
    wins = jnp.sum(prob[:, :, None] * first + (1.0 - prob)[:, :, None] * second, axis=1)
    count = jnp.sum(first + second, axis=1)
    winrate = (wins + 1.0) / (count + 2.0)
    placed = (owner[:, :, None] == numbers).astype(jnp.float32)
    rowrate = jnp.sum(winrate[:, :, None] * placed, axis=1).reshape(-1)
    coef = 2.0 * (logratio - eta_scale * (rowrate - 0.5))
    weighted = (
        (
            features.astype(jnp.float32).reshape(resp_dev, -1, features.shape[1])
            * coef[:, None, None]
        )
        .reshape(features.shape)
        .astype(jnp.bfloat16)
    )
    total_resp = resp_dev * n_dp
    full = lax.dot_general(
        weighted, attn_out, (((0,), (0,)), ((), ())), preferred_element_type=jnp.float32
    )
    full = full.astype(jnp.bfloat16).reshape(n_zl, n_plane, -1, full.shape[1])
    first_half = jnp.where(zl == 0, full[1], full[0])
    own_half = jnp.where(zl == 0, full[0], full[1])
    theirs = jnp.sum(lax.all_to_all(first_half, PLANE, 0, 0, tiled=True).astype(jnp.float32), axis=0)
    got = lax.ppermute(theirs, "zl", swap)
    shares = lax.all_to_all(own_half, PLANE, 0, 0, tiled=True)
    d_attn = jnp.dot(weighted, piece, preferred_element_type=jnp.float32).astype(jnp.bfloat16)
    shares, d_attn = lax.optimization_barrier((shares, d_attn))
    mine = jnp.sum(shares.astype(jnp.float32), axis=0)
    o_grad = (mine + got) / total_resp
    return (d_attn, o_grad)


def solution(mesh):
    n_zl = 2
    fine = Mesh(
        mesh.devices.reshape(
            n_zl, mesh.shape["dp"] // (n_zl * 4), 4, mesh.shape["tensor"] // 2, 2
        ),
        ("zl", "y", "x", "zh", "c"),
    )
    return jax.shard_map(
        shards,
        mesh=fine,
        in_specs=(
            P(DP, None),
            P(DP, None),
            P(DP, None, None),
            P(None, DP, TP),
            P(TP),
            P(TP),
            P(DP),
            P(DP, TP),
            P(DP, TP),
            P(DP, TP),
        ),
        out_specs=(P(DP, TP), P(DP, TP)),
        check_vma=False,
    )
```

```python
import jax
import jax.numpy as jnp
from jax import lax
from jax.sharding import Mesh
from jax.sharding import PartitionSpec as P

eta_scale = 2.0

DP = ("zl", "y", "x")
TP = ("zh", "c")
PLANE = ("y", "x")


def shards(
    embeds, owner, pairs, pref_weight, pref_bias, pref_out, logratio, attn_out, grad_out, w_out
):
    resp_dev = embeds.shape[0]
    prompts_dev = owner.shape[0]
    groups = owner.shape[1]
    npairs = pairs.shape[1]
    width_local = pref_weight.shape[2]
    rows_w = pref_weight.shape[1]
    n_dp = lax.axis_size(DP)
    n_zl = lax.axis_size("zl")
    n_plane = lax.axis_size(PLANE)
    zl = lax.axis_index("zl")
    swap = [(k, (k + 1) % n_zl) for k in range(n_zl)]
    features = lax.all_gather(grad_out, TP, axis=1, tiled=True)
    w_other = lax.ppermute(w_out, "zl", swap)
    other = lax.ppermute(pref_weight, "zl", swap)
    shape = (n_plane, 2) + w_out.shape
    first_w = jnp.broadcast_to(jnp.where(zl == 0, w_out, w_other)[None, None], shape)
    second_w = jnp.broadcast_to(jnp.where(zl == 0, w_other, w_out)[None, None], shape)
    copies = jnp.where(jnp.arange(2)[None, :, None, None] == 0, first_w, second_w)
    piece = lax.all_to_all(copies, PLANE, 0, 0, tiled=True)
    piece = piece.transpose(1, 0, 2, 3).reshape(-1, w_out.shape[1])

    pair_w = jnp.where(
        zl == 0,
        jnp.concatenate([pref_weight, other], axis=1),
        jnp.concatenate([other, pref_weight], axis=1),
    )
    cols = embeds.reshape(resp_dev, n_zl, n_plane, rows_w).transpose(2, 0, 1, 3)
    cols = cols.reshape(n_plane, resp_dev * n_zl * rows_w // 128, 128)
    cols = lax.all_to_all(cols, PLANE, 0, 0, tiled=True).reshape(n_plane * resp_dev, n_zl * rows_w)
    part = jnp.concatenate(
        [
            jnp.dot(cols, pair_w[0], preferred_element_type=jnp.float32),
            jnp.dot(cols, pair_w[1], preferred_element_type=jnp.float32),
        ],
        axis=1,
    )
    part = part.reshape(n_plane, resp_dev, part.shape[1])
    proj = jnp.sum(lax.all_to_all(part, PLANE, 0, 0, tiled=True), axis=0)

    base = (jnp.arange(prompts_dev, dtype=jnp.int32) * groups)[:, None]
    row_a = base + jnp.take_along_axis(owner, pairs[:, :, 0], axis=1)
    row_b = base + jnp.take_along_axis(owner, pairs[:, :, 1], axis=1)
    upper = proj[:, :width_local][row_a.reshape(-1)]
    lower = proj[:, width_local:][row_b.reshape(-1)]
    pre = (upper + lower).reshape(prompts_dev, npairs, width_local)
    hidden = jax.nn.gelu(pre + pref_bias)
    partial_logit = jnp.sum(hidden * pref_out, axis=-1)
    logit = lax.psum(partial_logit, TP)
    prob = jax.nn.sigmoid(logit)
    numbers = jnp.arange(groups, dtype=jnp.int32)
    first = (pairs[:, :, 0][:, :, None] == numbers).astype(jnp.float32)
    second = (pairs[:, :, 1][:, :, None] == numbers).astype(jnp.float32)
    wins = jnp.sum(prob[:, :, None] * first + (1.0 - prob)[:, :, None] * second, axis=1)
    count = jnp.sum(first + second, axis=1)
    winrate = (wins + 1.0) / (count + 2.0)
    placed = (owner[:, :, None] == numbers).astype(jnp.float32)
    rowrate = jnp.sum(winrate[:, :, None] * placed, axis=1).reshape(-1)
    coef = 2.0 * (logratio - eta_scale * (rowrate - 0.5))
    weighted = (
        (
            features.astype(jnp.float32).reshape(resp_dev, -1, features.shape[1])
            * coef[:, None, None]
        )
        .reshape(features.shape)
        .astype(jnp.bfloat16)
    )
    total_resp = resp_dev * n_dp
    full = lax.dot_general(
        weighted, attn_out, (((0,), (0,)), ((), ())), preferred_element_type=jnp.float32
    )
    full = full.astype(jnp.bfloat16).reshape(n_zl, n_plane, -1, full.shape[1])
    first_half = jnp.where(zl == 0, full[1], full[0])
    own_half = jnp.where(zl == 0, full[0], full[1])
    theirs = jnp.sum(lax.all_to_all(first_half, PLANE, 0, 0, tiled=True).astype(jnp.float32), axis=0)
    got = lax.ppermute(theirs, "zl", swap)
    shares = lax.all_to_all(own_half, PLANE, 0, 0, tiled=True)
    d_attn = jnp.dot(weighted, piece, preferred_element_type=jnp.float32).astype(jnp.bfloat16)
    shares, d_attn = lax.optimization_barrier((shares, d_attn))
    mine = jnp.sum(shares.astype(jnp.float32), axis=0)
    o_grad = (mine + got) / total_resp
    return (d_attn, o_grad)


def solution(mesh):
    n_zl = 2
    fine = Mesh(
        mesh.devices.reshape(
            n_zl, mesh.shape["dp"] // (n_zl * 4), 4, mesh.shape["tensor"] // 2, 2
        ),
        ("zl", "y", "x", "zh", "c"),
    )
    return jax.shard_map(
        shards,
        mesh=fine,
        in_specs=(
            P(DP, None),
            P(DP, None),
            P(DP, None, None),
            P(None, DP, TP),
            P(TP),
            P(TP),
            P(DP),
            P(DP, TP),
            P(DP, TP),
            P(DP, TP),
        ),
        out_specs=(P(DP, TP), P(DP, TP)),
        check_vma=False,
    )
```
